512 devices in a mesh: req: 64 (over x, z, core), tp: 8 (over y).
Axes of the slice: x: 4, y: 8, z: 8, core: 2. Of those that a mesh axis runs over, the one named last changes fastest.
Arguments:
- residual_input: bfloat16 [8192, 3584], P('req', 'tp'), may hold values from -6 to 6
- new_token_queries: bfloat16 [8192, 4096], P('req', 'tp'), may hold values from -8 to 8
- new_token_keys: bfloat16 [8192, 2048], P('req', 'tp'), may hold values from -8 to 8
- new_token_values: bfloat16 [8192, 2048], P('req', 'tp'), may hold values from -6 to 6
- key_page_pool: bfloat16 [1536, 16, 2048], P('req', None, 'tp'), may hold values from -6 to 6
- value_page_pool: bfloat16 [1536, 16, 2048], P('req', None, 'tp'), may hold values from -6 to 6
- request_page_table: int32 [128, 64], P('req'), may hold values from -1 to 23, as said below
- page_token_length: int32 [128, 64], P('req'), may hold values from 0 to 16, as said below
- request_token_length: int32 [64, 2], P('req'), may hold values from 1 to 96, 128 in all within a row
- request_adapter: int32 [64, 2], P('req'), may hold values from 0 to 63
- adapter_table_row: int32 [64], replicated, may hold values from 0 to 63, each once
- output_weight: bfloat16 [4096, 3584], P('tp'), may hold values from -0.125 to 0.125
- adapter_down_weight: bfloat16 [64, 16, 4096], P('req', None, 'tp'), may hold values from -0.09375 to 0.09375
- adapter_up_weight: bfloat16 [64, 16, 3584], P('req', None, 'tp'), may hold values from -1.5 to 1.5
- norm_scale_row: float32 [3584], P('tp'), may hold values from 0.25 to 1.75
Outputs:
- hidden_out: bfloat16 [8192, 3584], P('req', 'tp')
The draws below stay inside these ranges and needn't reach their ends.
Inputs may be any that keep to these rules, and one draw needn't show every extreme that they name: request_page_table[q, o] is a page of the pool of owner o (rows o * 24 to o * 24 + 23 of the pools), or -1; so the 2 requests of one index of req take at most 2 pages from one owner, and in every draw the requests of some index of req each take a page from every owner. Requests may share pages. `page_token_length`: 0 exactly where request_page_table is -1; every used page of a request is full but at most one.
All inputs are finite; a program needn't handle non-finite values.
Results may differ from the reference program's by a relative error of at most 0.015.
Values may be sent and summed in bfloat16 or wider, within the bound.
No kernel may reach another device: no remote copies, remote signals or barrier semaphores. Data moves between devices by JAX's collectives and lax.ppermute only.
A program may use at most 64 MiB of HBM per device.

```python
import math
import jax
import jax.numpy as jnp
import numpy as np
from jax import lax

MODEL_WIDTH = 3584
QUERY_HEADS = 16
VALUE_HEADS = 8
HEAD_SIZE = 256
ADAPTER_RANK = 16
PAGE_ROWS = 16
REQUEST_SHARE = 2
TOK_DEV = 128
PAGES_DEV = 24
TOKEN_COUNT = 8192
REQUESTS = 128
PAGE_COUNT = 1536
ADAPTER_COUNT = 64
N_REQ = 64
N_TP = 8


def page_layout(key):
    seeded = jax.random.fold_in(key, 11)
    key_level, key_full, key_roll, key_index, key_partial = jax.random.split(seeded, 5)
    levels = jax.random.randint(key_level, (N_REQ,), 1, 5)
    full_device = jax.random.randint(key_full, (), 0, N_REQ)
    rolled = jax.random.randint(key_roll, (N_REQ, REQUEST_SHARE, N_REQ), 0, 4)
    devices = jnp.arange(N_REQ)[:, None, None]
    used = (rolled < levels[:, None, None]) | (devices == full_device)
    indices = jax.random.randint(key_index, (N_REQ, REQUEST_SHARE, N_REQ), 0, PAGES_DEV)
    corner = (devices == full_device) & (jnp.arange(REQUEST_SHARE)[None, :, None] == 0) & (jnp.arange(N_REQ)[None, None, :] == 0)
    indices = jnp.where(corner, PAGES_DEV - 1, indices)
    owners = jnp.broadcast_to(jnp.arange(N_REQ)[None, None, :], used.shape)
    last_owner = jnp.max(jnp.where(used, owners, -1), axis=2)
    partial_fill = jax.random.randint(key_partial, (N_REQ, REQUEST_SHARE), 1, PAGE_ROWS + 1)
    filled = jnp.where(owners == last_owner[:, :, None], partial_fill[:, :, None], PAGE_ROWS)
    filled = jnp.where(used, filled, 0)
    table_rows = jnp.where(used, indices, -1)
    return (table_rows.reshape(REQUESTS, N_REQ).astype(jnp.int32), filled.reshape(REQUESTS, N_REQ).astype(jnp.int32))


def draw_request_page_table(key, part):
    return page_layout(key)[0]


def draw_page_token_length(key, part):
    return page_layout(key)[1]


def attention_inputs(key):
    seeded = jax.random.fold_in(key, 23)
    key_query, random_key_seed = jax.random.split(seeded, 2)
    query_rows = jnp.clip(jax.random.normal(key_query, (TOKEN_COUNT, QUERY_HEADS, HEAD_SIZE), jnp.float32), -6.0, 6.0)
    sampled_keys = jnp.clip(jax.random.normal(random_key_seed, (TOKEN_COUNT, VALUE_HEADS, HEAD_SIZE), jnp.float32), -6.0, 6.0)
    return (query_rows.reshape(TOKEN_COUNT, QUERY_HEADS * HEAD_SIZE), sampled_keys.reshape(TOKEN_COUNT, VALUE_HEADS * HEAD_SIZE))


def draw_new_token_queries(key, part):
    return attention_inputs(key)[0].astype(jnp.bfloat16)


def draw_new_token_keys(key, part):
    return attention_inputs(key)[1].astype(jnp.bfloat16)


def set_ends(entries, key, low, largest):
    extent = entries.shape
    index_at = [jax.random.randint(jax.random.fold_in(key, axis), (), 0, extent[axis]) for axis in range(len(extent))]
    entries = entries.at[tuple(index_at)].set(low)
    longest = extent.index(max(extent))
    index_at[longest] = (index_at[longest] + 1) % extent[longest]
    return entries.at[tuple(index_at)].set(largest)


def with_spikes(entries, key, source, target, parts, factor):
    def block_of(axis_at):
        return (jnp.arange(entries.shape[axis_at]) // (entries.shape[axis_at] // parts)).reshape((-1,) + (1,) * (entries.ndim - 1 - axis_at))

    first = jax.random.permutation(key, parts)[block_of(target)]
    other_side = (block_of(target) + parts // 2) % parts
    return jnp.where((block_of(source) == first) | (block_of(source) == other_side), factor * entries, entries)


def level_of(stream_key, dims, shards, smallest, largest):
    gain, own = 1.0, jax.random.fold_in(stream_key, 6)
    for dim, blocks in shards:
        draws = jnp.exp(jax.random.uniform(jax.random.fold_in(own, dim), (blocks,), jnp.float32, smallest / len(shards), largest / len(shards)))
        gain = gain * jnp.repeat(draws, dims[dim] // blocks).reshape([-1 if axis == dim else 1 for axis in range(len(dims))])
    return gain


def cumulative_ranks(number_of, lean):
    portions = [(1 << 20) // math.isqrt(standing ** lean) + 1 for standing in range(1, number_of + 1)]
    deviation = 1 + sum(portions) // (1 << 30)
    return np.cumsum(np.array([max(1, weight // deviation) for weight in portions]))


def skewed_ids(rng, dims, count, skew):
    table = cumulative_ranks(count, skew)
    ticket = jax.random.randint(jax.random.fold_in(rng, 1), dims, 0, int(table[count - 1]))
    standing = jnp.searchsorted(jnp.asarray(table, jnp.int32), ticket, side="right")
    return jax.random.permutation(jax.random.fold_in(rng, 2), count)[standing].astype(jnp.int32)


def split_up(count, total, bound, lean):
    weights = [(1 << 20) // math.isqrt(standing ** lean) + 1 for standing in range(2, count + 1)]
    rest, given = total - bound - (count - 1), [1] * (count - 1)
    while rest > 0:
        candidates = [i for i in range(count - 1) if given[i] < bound]
        whole, budget = sum([weights[i] for i in candidates]), rest
        for i in candidates:
            addition = min(bound - given[i], max(1, budget * weights[i] // whole), rest)
            given[i] = given[i] + addition
            rest = rest - addition
    return np.array([bound] + given)


def uneven_parts(key, number_of, total, bound, lean):
    if number_of == 2:
        one = jax.random.randint(key, (), max(1, total - bound), min(bound, total - 1) + 1)
        return jnp.stack([one, total - one])
    tallies = jnp.asarray(split_up(number_of, total, bound, lean), jnp.int32)
    pairs = (number_of - 1) // 2
    source_of, taker = tallies[1:1 + 2 * pairs:2], tallies[2:2 + 2 * pairs:2]
    margin = jnp.minimum(source_of - 1, bound - taker)
    passed = jax.random.randint(jax.random.fold_in(key, 1), (pairs,), 0, 1 << 20) % (margin + 1)
    tallies = tallies.at[1:1 + 2 * pairs:2].set(source_of - passed).at[2:2 + 2 * pairs:2].set(taker + passed)
    return tallies[jax.random.permutation(jax.random.fold_in(key, 2), number_of)]


def centred(rng, dims, spread, bound, cuts=(), kind=jnp.bfloat16):
    result = spread * jax.random.normal(rng, dims, jnp.float32)
    if cuts:
        result = result * level_of(rng, dims, cuts, -0.22, 0.18)
    return jnp.clip(result, -bound, bound).astype(kind)


def bell_draw_with(stream_key, extent, scale, limit, cuts, heavy, held_as=jnp.bfloat16):
    result = scale * jax.random.normal(stream_key, extent, jnp.float32)
    if cuts:
        result = result * level_of(stream_key, extent, cuts, -0.22, 0.18)
    return jnp.clip(with_spikes(result, jax.random.fold_in(stream_key, 3), *heavy), -limit, limit).astype(held_as)


def setup_inputs(seed: int = 0) -> dict:
    streams_of = jax.random.split(jax.random.key(seed), 16)
    return {
        "residual_input": centred(streams_of[0], (TOKEN_COUNT, MODEL_WIDTH), 1.0, 6.0, ((0, 64), (1, 8))),
        "new_token_queries": draw_new_token_queries(jax.random.fold_in(streams_of[15], 71), 0),
        "new_token_keys": draw_new_token_keys(jax.random.fold_in(streams_of[15], 71), 0),
        "new_token_values": centred(streams_of[3], (TOKEN_COUNT, VALUE_HEADS * HEAD_SIZE), 1.0, 6.0, ((0, 64), (1, 8))),
        "key_page_pool": centred(streams_of[4], (PAGE_COUNT, PAGE_ROWS, VALUE_HEADS * HEAD_SIZE), 1.0, 6.0, ((0, 64), (2, 8))),
        "value_page_pool": centred(streams_of[5], (PAGE_COUNT, PAGE_ROWS, VALUE_HEADS * HEAD_SIZE), 1.0, 6.0, ((0, 64), (2, 8))),
        "request_page_table": draw_request_page_table(jax.random.fold_in(streams_of[15], 71), 0),
        "page_token_length": draw_page_token_length(jax.random.fold_in(streams_of[15], 71), 0),
        "request_token_length": jax.vmap(lambda own: uneven_parts(own, REQUEST_SHARE, TOK_DEV, TOK_DEV * 3 // 4, 2))(jax.random.split(streams_of[8], N_REQ)).reshape((N_REQ, REQUEST_SHARE)).astype(jnp.int32),
        "request_adapter": set_ends(skewed_ids(streams_of[9], (N_REQ, REQUEST_SHARE), ADAPTER_COUNT, 2), jax.random.fold_in(streams_of[9], 3), 0, ADAPTER_COUNT - 1).astype(jnp.int32),
        "adapter_table_row": jax.random.permutation(streams_of[10], ADAPTER_COUNT).astype(jnp.int32),
        "output_weight": bell_draw_with(streams_of[11], (QUERY_HEADS * HEAD_SIZE, MODEL_WIDTH), (QUERY_HEADS * HEAD_SIZE) ** -0.5, 0.125, ((0, 8),), (0, 1, 8, 2.0)),
        "adapter_down_weight": centred(streams_of[12], (ADAPTER_COUNT, ADAPTER_RANK, QUERY_HEADS * HEAD_SIZE), (QUERY_HEADS * HEAD_SIZE) ** -0.5, 0.09375, ((0, 64), (2, 8))),
        "adapter_up_weight": centred(streams_of[13], (ADAPTER_COUNT, ADAPTER_RANK, MODEL_WIDTH), ADAPTER_RANK ** -0.5, 1.5, ((0, 64), (2, 8))),
        "norm_scale_row": jnp.clip(1.0 + 0.15 * jax.random.normal(streams_of[14], (MODEL_WIDTH,), jnp.float32), 0.25, 1.75),
    }


epsilon = 1e-06
adapter_scale = 2.0
masked_score = -1e+30

def attend(query_rows, new_keys, new_values, gathered_keys, gathered_values, usable, prompt_lengths):
    token_count = query_rows.shape[0]
    kv_heads = new_keys.shape[1] // HEAD_SIZE
    group_size = query_rows.shape[1] // new_keys.shape[1]
    requests_here = gathered_keys.shape[0]
    cached_count = gathered_keys.shape[1]
    query_heads = query_rows.astype(jnp.float32).reshape(token_count, kv_heads, group_size, HEAD_SIZE)
    past_keys = gathered_keys.astype(jnp.float32).reshape(requests_here, cached_count, kv_heads, HEAD_SIZE)
    past_values = gathered_values.astype(jnp.float32).reshape(requests_here * cached_count, kv_heads, HEAD_SIZE)
    fresh_keys = new_keys.astype(jnp.float32).reshape(token_count, kv_heads, HEAD_SIZE)
    fresh_values = new_values.astype(jnp.float32).reshape(token_count, kv_heads, HEAD_SIZE)
    positions = jnp.arange(token_count, dtype=jnp.int32)
    ends = jnp.cumsum(prompt_lengths).astype(jnp.int32)
    owner_request = lax.optimization_barrier(jnp.sum((positions[:, None] >= ends[None, :]).astype(jnp.int32), axis=1))
    scaling = HEAD_SIZE ** (-0.5)
    past_scores = jnp.einsum('tgqd,rngd->tgqrn', query_heads, past_keys) * scaling
    past_mask = usable[None, :, :] & (owner_request[:, None, None] == jnp.arange(requests_here, dtype=jnp.int32)[None, :, None])
    past_scores = jnp.where(past_mask[:, None, None, :, :], past_scores, masked_score)
    past_scores = past_scores.reshape(token_count, kv_heads, group_size, requests_here * cached_count)
    fresh_scores = jnp.einsum('tgqd,ugd->tgqu', query_heads, fresh_keys) * scaling
    fresh_mask = (owner_request[:, None] == owner_request[None, :]) & (positions[None, :] <= positions[:, None])
    fresh_scores = jnp.where(fresh_mask[:, None, None, :], fresh_scores, masked_score)
    scores = jnp.concatenate([past_scores, fresh_scores], axis=3)
    highest = lax.optimization_barrier(jnp.max(scores, axis=3, keepdims=True))
    weights = jnp.exp(scores - highest)
    weights = (weights / lax.optimization_barrier(jnp.sum(weights, axis=3, keepdims=True))).astype(jnp.bfloat16)
    all_values = jnp.concatenate([past_values, fresh_values], axis=0)
    mixed = jnp.einsum('tgqk,kgd->tgqd', weights.astype(jnp.float32), all_values)
    return mixed.reshape(token_count, -1).astype(jnp.bfloat16)

def reference(residual_input, new_token_queries, new_token_keys, new_token_values, key_page_pool, value_page_pool, request_page_table, page_token_length, request_token_length, request_adapter, adapter_table_row, output_weight, adapter_down_weight, adapter_up_weight, norm_scale_row):
    head_part = QUERY_HEADS * HEAD_SIZE // N_TP

    def one_block(index):
        first_row = index * TOK_DEV
        query_rows = lax.dynamic_slice_in_dim(new_token_queries, first_row, TOK_DEV, 0)
        new_keys = lax.dynamic_slice_in_dim(new_token_keys, first_row, TOK_DEV, 0)
        new_values = lax.dynamic_slice_in_dim(new_token_values, first_row, TOK_DEV, 0)
        hidden_rows = lax.dynamic_slice_in_dim(residual_input, first_row, TOK_DEV, 0)
        table_rows = lax.dynamic_slice_in_dim(request_page_table, index * REQUEST_SHARE, REQUEST_SHARE, 0)
        filled = lax.dynamic_slice_in_dim(page_token_length, index * REQUEST_SHARE, REQUEST_SHARE, 0)
        page_position = jnp.arange(N_REQ, dtype=jnp.int32)[None, :] * PAGES_DEV + jnp.maximum(table_rows, 0)
        gathered_keys = key_page_pool[page_position].reshape(REQUEST_SHARE, N_REQ * PAGE_ROWS, VALUE_HEADS * HEAD_SIZE)
        gathered_values = value_page_pool[page_position].reshape(REQUEST_SHARE, N_REQ * PAGE_ROWS, VALUE_HEADS * HEAD_SIZE)
        usable = (jnp.arange(PAGE_ROWS, dtype=jnp.int32)[None, None, :] < filled[:, :, None]).reshape(REQUEST_SHARE, N_REQ * PAGE_ROWS)
        lengths = lax.dynamic_index_in_dim(request_token_length, index, 0, keepdims=False)
        attention = attend(query_rows, new_keys, new_values, gathered_keys, gathered_values, usable, lengths)
        chosen_pages = adapter_table_row[lax.dynamic_index_in_dim(request_adapter, index, 0, keepdims=False)]
        selected_input = adapter_down_weight[chosen_pages]
        selected_output = adapter_up_weight[chosen_pages]
        positions = jnp.arange(TOK_DEV, dtype=jnp.int32)
        ends = jnp.cumsum(lengths).astype(jnp.int32)
        owner_request = lax.optimization_barrier(jnp.sum((positions[:, None] >= ends[None, :]).astype(jnp.int32), axis=1))
        selector = (owner_request[:, None] == jnp.arange(REQUEST_SHARE, dtype=jnp.int32)[None, :]).astype(jnp.float32)
        base_output = jnp.zeros((TOK_DEV, MODEL_WIDTH), jnp.float32)
        low = jnp.zeros((TOK_DEV, ADAPTER_RANK), jnp.float32)
        for shard in range(N_TP):
            lower = shard * head_part
            part_cols = attention[:, lower:lower + head_part]
            term = jnp.dot(part_cols, output_weight[lower:lower + head_part], preferred_element_type=jnp.float32)
            base_output = base_output + lax.optimization_barrier(term.astype(jnp.bfloat16)).astype(jnp.float32)
            low_terms = jnp.einsum('tc,rkc->trk', part_cols.astype(jnp.float32), selected_input[:, :, lower:lower + head_part].astype(jnp.float32))
            low_part = lax.optimization_barrier(jnp.sum(low_terms * selector[:, :, None], axis=1))
            low = low + lax.optimization_barrier(low_part.astype(jnp.bfloat16)).astype(jnp.float32)
        low_rounded = low.astype(jnp.bfloat16)
        rows_masked = (low_rounded[:, None, :] * selector.astype(jnp.bfloat16)[:, :, None]).reshape(TOK_DEV, REQUEST_SHARE * ADAPTER_RANK)
        adapter_output = jnp.dot(rows_masked, selected_output.reshape(REQUEST_SHARE * ADAPTER_RANK, MODEL_WIDTH), preferred_element_type=jnp.float32)
        projected_rows = base_output + adapter_scale * adapter_output
        mean_square = lax.optimization_barrier(jnp.mean(projected_rows * projected_rows, axis=1, keepdims=True))
        scaled = projected_rows * lax.rsqrt(mean_square + epsilon) * norm_scale_row.astype(jnp.float32)
        return (hidden_rows.astype(jnp.float32) + scaled).astype(jnp.bfloat16)
    blocks = lax.map(one_block, jnp.arange(N_REQ, dtype=jnp.int32))
    return blocks.reshape(N_REQ * TOK_DEV, MODEL_WIDTH)
```

```python
import jax
import jax.numpy as jnp
from jax import lax
from jax.sharding import PartitionSpec as P

HEAD_SIZE = 256


epsilon = 1e-06
adapter_scale = 2.0
masked_score = -1e30


def attend(
    query_rows, new_keys, new_values, gathered_keys, gathered_values, usable, owner_request
):
    token_count = query_rows.shape[0]
    kv_heads = new_keys.shape[1] // HEAD_SIZE
    group_size = query_rows.shape[1] // new_keys.shape[1]
    requests_here = gathered_keys.shape[0]
    cached_count = gathered_keys.shape[1]
    query_heads = query_rows.reshape(token_count, kv_heads, group_size, HEAD_SIZE)
    past_keys = gathered_keys.reshape(requests_here, cached_count, kv_heads, HEAD_SIZE)
    past_values = gathered_values.reshape(requests_here * cached_count, kv_heads, HEAD_SIZE)
    fresh_keys = new_keys.reshape(token_count, kv_heads, HEAD_SIZE)
    fresh_values = new_values.reshape(token_count, kv_heads, HEAD_SIZE)
    positions = jnp.arange(token_count, dtype=jnp.int32)
    scaling = HEAD_SIZE ** (-0.5)
    past_scores = (
        jnp.einsum("tgqd,rngd->tgqrn", query_heads, past_keys, preferred_element_type=jnp.float32)
        * scaling
    )
    past_mask = usable[None, :, :] & (
        owner_request[:, None, None] == jnp.arange(requests_here, dtype=jnp.int32)[None, :, None]
    )
    past_scores = jnp.where(past_mask[:, None, None, :, :], past_scores, masked_score)
    past_scores = past_scores.reshape(
        token_count, kv_heads, group_size, requests_here * cached_count
    )
    fresh_scores = (
        jnp.einsum("tgqd,ugd->tgqu", query_heads, fresh_keys, preferred_element_type=jnp.float32)
        * scaling
    )
    fresh_mask = (owner_request[:, None] == owner_request[None, :]) & (
        positions[None, :] <= positions[:, None]
    )
    fresh_scores = jnp.where(fresh_mask[:, None, None, :], fresh_scores, masked_score)
    scores = jnp.concatenate([past_scores, fresh_scores], axis=3)
    highest = jnp.max(scores, axis=3, keepdims=True)
    weights = jnp.exp(scores - highest)
    weights = (weights / jnp.sum(weights, axis=3, keepdims=True)).astype(jnp.bfloat16)
    all_values = jnp.concatenate([past_values, fresh_values], axis=0)
    mixed = jnp.einsum("tgqk,kgd->tgqd", weights, all_values, preferred_element_type=jnp.float32)
    return mixed.reshape(token_count, -1).astype(jnp.bfloat16)


def local(
    residual_input,
    new_token_queries,
    new_token_keys,
    new_token_values,
    key_page_pool,
    value_page_pool,
    request_page_table,
    page_token_length,
    request_token_length,
    request_adapter,
    adapter_table_row,
    output_weight,
    adapter_down_weight,
    adapter_up_weight,
    norm_scale_row,
):
    owners = lax.axis_size("req")
    groups = lax.axis_size("tp")
    requests_here = request_page_table.shape[0]
    page_rows = key_page_pool.shape[1]
    token_count = new_token_queries.shape[0]
    width_part = residual_input.shape[1]
    head_cols = key_page_pool.shape[2]
    down_cols = adapter_down_weight.shape[2]

    adapter_pair = jnp.concatenate([adapter_down_weight, adapter_up_weight], axis=2)
    adapters_everywhere = lax.all_gather(adapter_pair, "req", axis=0, tiled=True)

    wanted = lax.all_to_all(request_page_table, "req", split_axis=1, concat_axis=1, tiled=True)
    page_picks = jnp.maximum(wanted, 0)
    kv_pool = jnp.concatenate([key_page_pool, value_page_pool], axis=2)
    kv_out = kv_pool[page_picks]
    kv_back = lax.all_to_all(kv_out, "req", split_axis=1, concat_axis=1, tiled=True)
    kv_back = kv_back.reshape(requests_here, owners * page_rows, 2 * head_cols)
    gathered_keys = kv_back[:, :, :head_cols]
    gathered_values = kv_back[:, :, head_cols:]
    usable = (
        jnp.arange(page_rows, dtype=jnp.int32)[None, None, :] < page_token_length[:, :, None]
    ).reshape(requests_here, owners * page_rows)
    lengths = request_token_length[0]
    positions = jnp.arange(token_count, dtype=jnp.int32)
    ends = jnp.cumsum(lengths)
    owner_request = jnp.sum((positions[:, None] >= ends[None, :]).astype(jnp.int32), axis=1)
    attention = attend(
        new_token_queries,
        new_token_keys,
        new_token_values,
        gathered_keys,
        gathered_values,
        usable,
        owner_request,
    )

    adapters_all = adapter_table_row.shape[0]
    matches = request_adapter[0][:, None] == jnp.arange(adapters_all, dtype=jnp.int32)[None, :]
    chosen_pages = jnp.sum(jnp.where(matches, adapter_table_row[None, :], 0), axis=1)
    rows_here = adapters_everywhere.shape[0]
    picker = (chosen_pages[:, None] == jnp.arange(rows_here, dtype=jnp.int32)[None, :]).astype(
        jnp.bfloat16
    )
    selected = jnp.einsum(
        "rk,kab->rab", picker, adapters_everywhere, preferred_element_type=jnp.float32
    ).astype(jnp.bfloat16)
    adapter_in = selected[:, :, :down_cols]
    adapter_out = selected[:, :, down_cols:]
    rank_size = adapter_in.shape[1]

    selector = (
        owner_request[:, None] == jnp.arange(requests_here, dtype=jnp.int32)[None, :]
    ).astype(jnp.float32)
    selector_half = selector.astype(jnp.bfloat16)
    base_part = jnp.dot(attention, output_weight, preferred_element_type=jnp.float32)
    low_terms = jnp.einsum("tc,rkc->trk", attention, adapter_in, preferred_element_type=jnp.float32)
    low_part = jnp.sum(low_terms * selector[:, :, None], axis=1)

    base_slots = base_part.astype(jnp.bfloat16).reshape(token_count, groups, width_part)
    base_slots = jnp.transpose(base_slots, (1, 0, 2))
    low_slots = jnp.broadcast_to(
        low_part.astype(jnp.bfloat16)[None], (groups, token_count, rank_size)
    )
    pad_cols = (-(width_part + rank_size)) % 128
    slots = jnp.concatenate(
        [base_slots, low_slots, jnp.zeros((groups, token_count, pad_cols), jnp.bfloat16)], axis=2
    )
    arrived = lax.all_to_all(slots, "tp", split_axis=0, concat_axis=0, tiled=True)
    arrived = arrived.astype(jnp.float32)
    base_local = jnp.sum(arrived[:, :, :width_part], axis=0)
    low_sum = jnp.sum(arrived[:, :, width_part:width_part + rank_size], axis=0)

    rows_masked = (low_sum.astype(jnp.bfloat16)[:, None, :] * selector_half[:, :, None]).reshape(
        token_count, requests_here * rank_size
    )
    projected = base_local + adapter_scale * jnp.dot(
        rows_masked,
        adapter_out.reshape(requests_here * rank_size, width_part),
        preferred_element_type=jnp.float32,
    )
    square_part = jnp.sum(projected * projected, axis=1)
    square_sum = lax.psum(square_part, "tp")
    mean_square = square_sum / (groups * width_part)
    scaled = projected * lax.rsqrt(mean_square + epsilon)[:, None]
    return (residual_input.astype(jnp.float32) + scaled * norm_scale_row).astype(jnp.bfloat16)


def solution(mesh):
    in_specs = (
        P("req", "tp"),
        P("req", "tp"),
        P("req", "tp"),
        P("req", "tp"),
        P("req", None, "tp"),
        P("req", None, "tp"),
        P("req", None),
        P("req", None),
        P("req", None),
        P("req", None),
        P(),
        P("tp", None),
        P("req", None, "tp"),
        P("req", None, "tp"),
        P("tp"),
    )
    out_specs = P("req", "tp")
    return jax.shard_map(local, mesh=mesh, in_specs=in_specs, out_specs=out_specs, check_vma=False)
```

```python
import jax
import jax.numpy as jnp
from jax import lax
from jax.sharding import PartitionSpec as P

HEAD_SIZE = 256
KV_OWNER_MAJOR = True
TP_TRANSPOSED = True
INDEX_TRANSPOSED = True


epsilon = 1e-06
adapter_scale = 2.0
masked_score = -1e30


def attend(
    query_rows, new_keys, new_values, gathered_keys, gathered_values, usable, owner_request
):
    token_count = query_rows.shape[0]
    kv_heads = new_keys.shape[1] // HEAD_SIZE
    group_size = query_rows.shape[1] // new_keys.shape[1]
    requests_here = gathered_keys.shape[0]
    cached_count = gathered_keys.shape[1]
    query_heads = query_rows.reshape(token_count, kv_heads, group_size, HEAD_SIZE)
    past_keys = gathered_keys.reshape(requests_here, cached_count, kv_heads, HEAD_SIZE)
    past_values = gathered_values.reshape(requests_here * cached_count, kv_heads, HEAD_SIZE)
    fresh_keys = new_keys.reshape(token_count, kv_heads, HEAD_SIZE)
    fresh_values = new_values.reshape(token_count, kv_heads, HEAD_SIZE)
    positions = jnp.arange(token_count, dtype=jnp.int32)
    scaling = HEAD_SIZE ** (-0.5)
    past_scores = (
        jnp.einsum("tgqd,rngd->tgqrn", query_heads, past_keys, preferred_element_type=jnp.float32)
        * scaling
    )
    past_mask = usable[None, :, :] & (
        owner_request[:, None, None] == jnp.arange(requests_here, dtype=jnp.int32)[None, :, None]
    )
    past_scores = jnp.where(past_mask[:, None, None, :, :], past_scores, masked_score)
    past_scores = past_scores.reshape(
        token_count, kv_heads, group_size, requests_here * cached_count
    )
    fresh_scores = (
        jnp.einsum("tgqd,ugd->tgqu", query_heads, fresh_keys, preferred_element_type=jnp.float32)
        * scaling
    )
    fresh_mask = (owner_request[:, None] == owner_request[None, :]) & (
        positions[None, :] <= positions[:, None]
    )
    fresh_scores = jnp.where(fresh_mask[:, None, None, :], fresh_scores, masked_score)
    scores = jnp.concatenate([past_scores, fresh_scores], axis=3)
    highest = jnp.max(scores, axis=3, keepdims=True)
    weights = jnp.exp(scores - highest)
    weights = (weights / jnp.sum(weights, axis=3, keepdims=True)).astype(jnp.bfloat16)
    all_values = jnp.concatenate([past_values, fresh_values], axis=0)
    mixed = jnp.einsum("tgqk,kgd->tgqd", weights, all_values, preferred_element_type=jnp.float32)
    return mixed.reshape(token_count, -1).astype(jnp.bfloat16)


def attend_flat(query_rows, new_keys, new_values, past_keys, past_values, past_mask, owner_request):
    token_count = query_rows.shape[0]
    kv_heads = new_keys.shape[1] // HEAD_SIZE
    group_size = query_rows.shape[1] // new_keys.shape[1]
    query_heads = query_rows.reshape(token_count, kv_heads, group_size, HEAD_SIZE)
    fresh_keys = new_keys.reshape(token_count, kv_heads, HEAD_SIZE)
    fresh_values = new_values.reshape(token_count, kv_heads, HEAD_SIZE)
    positions = jnp.arange(token_count, dtype=jnp.int32)
    scaling = HEAD_SIZE ** (-0.5)
    past_scores = (
        jnp.einsum("tgqd,kgd->tgqk", query_heads, past_keys, preferred_element_type=jnp.float32)
        * scaling
    )
    past_scores = jnp.where(past_mask[:, None, None, :], past_scores, masked_score)
    fresh_scores = (
        jnp.einsum("tgqd,ugd->tgqu", query_heads, fresh_keys, preferred_element_type=jnp.float32)
        * scaling
    )
    fresh_mask = (owner_request[:, None] == owner_request[None, :]) & (
        positions[None, :] <= positions[:, None]
    )
    fresh_scores = jnp.where(fresh_mask[:, None, None, :], fresh_scores, masked_score)
    scores = jnp.concatenate([past_scores, fresh_scores], axis=3)
    highest = jnp.max(scores, axis=3, keepdims=True)
    weights = jnp.exp(scores - highest)
    weights = (weights / jnp.sum(weights, axis=3, keepdims=True)).astype(jnp.bfloat16)
    all_values = jnp.concatenate([past_values, fresh_values], axis=0)
    mixed = jnp.einsum("tgqk,kgd->tgqd", weights, all_values, preferred_element_type=jnp.float32)
    return mixed.reshape(token_count, -1).astype(jnp.bfloat16)


def local(
    residual_input,
    new_token_queries,
    new_token_keys,
    new_token_values,
    key_page_pool,
    value_page_pool,
    request_page_table,
    page_token_length,
    request_token_length,
    request_adapter,
    adapter_table_row,
    output_weight,
    adapter_down_weight,
    adapter_up_weight,
    norm_scale_row,
):
    owners = lax.axis_size("req")
    groups = lax.axis_size("tp")
    requests_here = request_page_table.shape[0]
    page_rows = key_page_pool.shape[1]
    token_count = new_token_queries.shape[0]
    width_part = residual_input.shape[1]
    head_cols = key_page_pool.shape[2]
    down_cols = adapter_down_weight.shape[2]

    adapter_pair = jnp.concatenate([adapter_down_weight, adapter_up_weight], axis=2)
    adapters_everywhere = lax.all_gather(adapter_pair, "req", axis=0, tiled=True)

    if INDEX_TRANSPOSED:
        wanted = lax.all_to_all(request_page_table.T, "req", split_axis=0, concat_axis=0, tiled=True).T
    else:
        wanted = lax.all_to_all(request_page_table, "req", split_axis=1, concat_axis=1, tiled=True)
    page_picks = jnp.maximum(wanted, 0)
    kv_pool = jnp.concatenate([key_page_pool, value_page_pool], axis=2)
    lengths = request_token_length[0]
    positions = jnp.arange(token_count, dtype=jnp.int32)
    ends = jnp.cumsum(lengths)
    owner_request = jnp.sum((positions[:, None] >= ends[None, :]).astype(jnp.int32), axis=1)
    kv_heads = head_cols // HEAD_SIZE
    if KV_OWNER_MAJOR:
        kv_out = kv_pool[page_picks.T]
        kv_back = lax.all_to_all(kv_out, "req", split_axis=0, concat_axis=0, tiled=True)
        cached = owners * requests_here * page_rows
        past_keys = kv_back[..., :head_cols].reshape(cached, kv_heads, HEAD_SIZE)
        past_values = kv_back[..., head_cols:].reshape(cached, kv_heads, HEAD_SIZE)
        row_used = (
            jnp.arange(page_rows, dtype=jnp.int32)[None, None, :] < page_token_length.T[:, :, None]
        )
        request_match = owner_request[:, None] == jnp.arange(requests_here, dtype=jnp.int32)[None, :]
        past_mask = (row_used[None] & request_match[:, None, :, None]).reshape(token_count, cached)
        attention = attend_flat(
            new_token_queries,
            new_token_keys,
            new_token_values,
            past_keys,
            past_values,
            past_mask,
            owner_request,
        )
    else:
        kv_out = kv_pool[page_picks]
        kv_back = lax.all_to_all(kv_out, "req", split_axis=1, concat_axis=1, tiled=True)
        kv_back = kv_back.reshape(requests_here, owners * page_rows, 2 * head_cols)
        gathered_keys = kv_back[:, :, :head_cols]
        gathered_values = kv_back[:, :, head_cols:]
        usable = (
            jnp.arange(page_rows, dtype=jnp.int32)[None, None, :] < page_token_length[:, :, None]
        ).reshape(requests_here, owners * page_rows)
        attention = attend(
            new_token_queries,
            new_token_keys,
            new_token_values,
            gathered_keys,
            gathered_values,
            usable,
            owner_request,
        )

    adapters_all = adapter_table_row.shape[0]
    matches = request_adapter[0][:, None] == jnp.arange(adapters_all, dtype=jnp.int32)[None, :]
    chosen_pages = jnp.sum(jnp.where(matches, adapter_table_row[None, :], 0), axis=1)
    rows_here = adapters_everywhere.shape[0]
    picker = (chosen_pages[:, None] == jnp.arange(rows_here, dtype=jnp.int32)[None, :]).astype(
        jnp.bfloat16
    )
    selected = jnp.einsum(
        "rk,kab->rab", picker, adapters_everywhere, preferred_element_type=jnp.float32
    ).astype(jnp.bfloat16)
    adapter_in = selected[:, :, :down_cols]
    adapter_out = selected[:, :, down_cols:]
    rank_size = adapter_in.shape[1]

    selector = (
        owner_request[:, None] == jnp.arange(requests_here, dtype=jnp.int32)[None, :]
    ).astype(jnp.float32)
    selector_half = selector.astype(jnp.bfloat16)
    base_part = jnp.dot(attention, output_weight, preferred_element_type=jnp.float32)
    low_terms = jnp.einsum("tc,rkc->trk", attention, adapter_in, preferred_element_type=jnp.float32)
    low_part = jnp.sum(low_terms * selector[:, :, None], axis=1)

    if TP_TRANSPOSED:
        base_t = jnp.einsum("tc,cw->wt", attention, output_weight, preferred_element_type=jnp.float32)
        base_slots = base_t.astype(jnp.bfloat16).reshape(groups, width_part, token_count)
        low_slots = jnp.broadcast_to(
            low_part.astype(jnp.bfloat16).T[None], (groups, rank_size, token_count)
        )
        slots = jnp.concatenate([base_slots, low_slots], axis=1)
        arrived = lax.all_to_all(slots, "tp", split_axis=0, concat_axis=0, tiled=True)
        arrived = jnp.sum(arrived.astype(jnp.float32), axis=0)
        base_local = arrived[:width_part].T
        low_sum = arrived[width_part:width_part + rank_size].T
    else:
        base_slots = base_part.astype(jnp.bfloat16).reshape(token_count, groups, width_part)
        base_slots = jnp.transpose(base_slots, (1, 0, 2))
        low_slots = jnp.broadcast_to(
            low_part.astype(jnp.bfloat16)[None], (groups, token_count, rank_size)
        )
        pad_cols = (-(width_part + rank_size)) % 128
        slots = jnp.concatenate(
            [base_slots, low_slots, jnp.zeros((groups, token_count, pad_cols), jnp.bfloat16)], axis=2
        )
        arrived = lax.all_to_all(slots, "tp", split_axis=0, concat_axis=0, tiled=True)
        arrived = arrived.astype(jnp.float32)
        base_local = jnp.sum(arrived[:, :, :width_part], axis=0)
        low_sum = jnp.sum(arrived[:, :, width_part:width_part + rank_size], axis=0)

    rows_masked = (low_sum.astype(jnp.bfloat16)[:, None, :] * selector_half[:, :, None]).reshape(
        token_count, requests_here * rank_size
    )
    projected = base_local + adapter_scale * jnp.dot(
        rows_masked,
        adapter_out.reshape(requests_here * rank_size, width_part),
        preferred_element_type=jnp.float32,
    )
    square_part = jnp.sum(projected * projected, axis=1)
    square_sum = lax.psum(square_part, "tp")
    mean_square = square_sum / (groups * width_part)
    scaled = projected * lax.rsqrt(mean_square + epsilon)[:, None]
    return (residual_input.astype(jnp.float32) + scaled * norm_scale_row).astype(jnp.bfloat16)


def solution(mesh):
    in_specs = (
        P("req", "tp"),
        P("req", "tp"),
        P("req", "tp"),
        P("req", "tp"),
        P("req", None, "tp"),
        P("req", None, "tp"),
        P("req", None),
        P("req", None),
        P("req", None),
        P("req", None),
        P(),
        P("tp", None),
        P("req", None, "tp"),
        P("req", None, "tp"),
        P("tp"),
    )
    out_specs = P("req", "tp")
    return jax.shard_map(local, mesh=mesh, in_specs=in_specs, out_specs=out_specs, check_vma=False)
```

```python
import jax
import jax.numpy as jnp
from jax import lax
from jax.sharding import PartitionSpec as P

HEAD_SIZE = 256
SEPARATE_GATHER = False
KV_OWNER_MAJOR = True
TP_TRANSPOSED = True
INDEX_TRANSPOSED = True


epsilon = 1e-06
adapter_scale = 2.0
masked_score = -1e30


def attend(
    query_rows, new_keys, new_values, gathered_keys, gathered_values, usable, owner_request
):
    token_count = query_rows.shape[0]
    kv_heads = new_keys.shape[1] // HEAD_SIZE
    group_size = query_rows.shape[1] // new_keys.shape[1]
    requests_here = gathered_keys.shape[0]
    cached_count = gathered_keys.shape[1]
    query_heads = query_rows.reshape(token_count, kv_heads, group_size, HEAD_SIZE)
    past_keys = gathered_keys.reshape(requests_here, cached_count, kv_heads, HEAD_SIZE)
    past_values = gathered_values.reshape(requests_here * cached_count, kv_heads, HEAD_SIZE)
    fresh_keys = new_keys.reshape(token_count, kv_heads, HEAD_SIZE)
    fresh_values = new_values.reshape(token_count, kv_heads, HEAD_SIZE)
    positions = jnp.arange(token_count, dtype=jnp.int32)
    scaling = HEAD_SIZE ** (-0.5)
    past_scores = (
        jnp.einsum("tgqd,rngd->tgqrn", query_heads, past_keys, preferred_element_type=jnp.float32)
        * scaling
    )
    past_mask = usable[None, :, :] & (
        owner_request[:, None, None] == jnp.arange(requests_here, dtype=jnp.int32)[None, :, None]
    )
    past_scores = jnp.where(past_mask[:, None, None, :, :], past_scores, masked_score)
    past_scores = past_scores.reshape(
        token_count, kv_heads, group_size, requests_here * cached_count
    )
    fresh_scores = (
        jnp.einsum("tgqd,ugd->tgqu", query_heads, fresh_keys, preferred_element_type=jnp.float32)
        * scaling
    )
    fresh_mask = (owner_request[:, None] == owner_request[None, :]) & (
        positions[None, :] <= positions[:, None]
    )
    fresh_scores = jnp.where(fresh_mask[:, None, None, :], fresh_scores, masked_score)
    scores = jnp.concatenate([past_scores, fresh_scores], axis=3)
    highest = jnp.max(scores, axis=3, keepdims=True)
    weights = jnp.exp(scores - highest)
    weights = (weights / jnp.sum(weights, axis=3, keepdims=True)).astype(jnp.bfloat16)
    all_values = jnp.concatenate([past_values, fresh_values], axis=0)
    mixed = jnp.einsum("tgqk,kgd->tgqd", weights, all_values, preferred_element_type=jnp.float32)
    return mixed.reshape(token_count, -1).astype(jnp.bfloat16)


def attend_flat(query_rows, new_keys, new_values, past_keys, past_values, past_mask, owner_request):
    token_count = query_rows.shape[0]
    kv_heads = new_keys.shape[1] // HEAD_SIZE
    group_size = query_rows.shape[1] // new_keys.shape[1]
    query_heads = query_rows.reshape(token_count, kv_heads, group_size, HEAD_SIZE)
    fresh_keys = new_keys.reshape(token_count, kv_heads, HEAD_SIZE)
    fresh_values = new_values.reshape(token_count, kv_heads, HEAD_SIZE)
    positions = jnp.arange(token_count, dtype=jnp.int32)
    scaling = HEAD_SIZE ** (-0.5)
    past_scores = (
        jnp.einsum("tgqd,kgd->tgqk", query_heads, past_keys, preferred_element_type=jnp.float32)
        * scaling
    )
    past_scores = jnp.where(past_mask[:, None, None, :], past_scores, masked_score)
    fresh_scores = (
        jnp.einsum("tgqd,ugd->tgqu", query_heads, fresh_keys, preferred_element_type=jnp.float32)
        * scaling
    )
    fresh_mask = (owner_request[:, None] == owner_request[None, :]) & (
        positions[None, :] <= positions[:, None]
    )
    fresh_scores = jnp.where(fresh_mask[:, None, None, :], fresh_scores, masked_score)
    scores = jnp.concatenate([past_scores, fresh_scores], axis=3)
    highest = jnp.max(scores, axis=3, keepdims=True)
    weights = jnp.exp(scores - highest)
    weights = (weights / jnp.sum(weights, axis=3, keepdims=True)).astype(jnp.bfloat16)
    all_values = jnp.concatenate([past_values, fresh_values], axis=0)
    mixed = jnp.einsum("tgqk,kgd->tgqd", weights, all_values, preferred_element_type=jnp.float32)
    return mixed.reshape(token_count, -1).astype(jnp.bfloat16)


def local(
    residual_input,
    new_token_queries,
    new_token_keys,
    new_token_values,
    key_page_pool,
    value_page_pool,
    request_page_table,
    page_token_length,
    request_token_length,
    request_adapter,
    adapter_table_row,
    output_weight,
    adapter_down_weight,
    adapter_up_weight,
    norm_scale_row,
):
    owners = lax.axis_size("req")
    groups = lax.axis_size("tp")
    requests_here = request_page_table.shape[0]
    page_rows = key_page_pool.shape[1]
    token_count = new_token_queries.shape[0]
    width_part = residual_input.shape[1]
    head_cols = key_page_pool.shape[2]
    down_cols = adapter_down_weight.shape[2]

    if SEPARATE_GATHER:
        down_everywhere, up_everywhere = lax.all_gather(
            (adapter_down_weight, adapter_up_weight), "req", axis=0, tiled=True
        )
    else:
        adapter_pair = jnp.concatenate([adapter_down_weight, adapter_up_weight], axis=2)
        adapters_everywhere = lax.all_gather(adapter_pair, "req", axis=0, tiled=True)

    if INDEX_TRANSPOSED:
        wanted = lax.all_to_all(request_page_table.T, "req", split_axis=0, concat_axis=0, tiled=True).T
    else:
        wanted = lax.all_to_all(request_page_table, "req", split_axis=1, concat_axis=1, tiled=True)
    page_picks = jnp.maximum(wanted, 0)
    kv_pool = jnp.concatenate([key_page_pool, value_page_pool], axis=2)
    lengths = request_token_length[0]
    positions = jnp.arange(token_count, dtype=jnp.int32)
    ends = jnp.cumsum(lengths)
    owner_request = jnp.sum((positions[:, None] >= ends[None, :]).astype(jnp.int32), axis=1)
    kv_heads = head_cols // HEAD_SIZE
    if KV_OWNER_MAJOR:
        kv_out = kv_pool[page_picks.T]
        kv_back = lax.all_to_all(kv_out, "req", split_axis=0, concat_axis=0, tiled=True)
        cached = owners * requests_here * page_rows
        past_keys = kv_back[..., :head_cols].reshape(cached, kv_heads, HEAD_SIZE)
        past_values = kv_back[..., head_cols:].reshape(cached, kv_heads, HEAD_SIZE)
        row_used = (
            jnp.arange(page_rows, dtype=jnp.int32)[None, None, :] < page_token_length.T[:, :, None]
        )
        request_match = owner_request[:, None] == jnp.arange(requests_here, dtype=jnp.int32)[None, :]
        past_mask = (row_used[None] & request_match[:, None, :, None]).reshape(token_count, cached)
        attention = attend_flat(
            new_token_queries,
            new_token_keys,
            new_token_values,
            past_keys,
            past_values,
            past_mask,
            owner_request,
        )
    else:
        kv_out = kv_pool[page_picks]
        kv_back = lax.all_to_all(kv_out, "req", split_axis=1, concat_axis=1, tiled=True)
        kv_back = kv_back.reshape(requests_here, owners * page_rows, 2 * head_cols)
        gathered_keys = kv_back[:, :, :head_cols]
        gathered_values = kv_back[:, :, head_cols:]
        usable = (
            jnp.arange(page_rows, dtype=jnp.int32)[None, None, :] < page_token_length[:, :, None]
        ).reshape(requests_here, owners * page_rows)
        attention = attend(
            new_token_queries,
            new_token_keys,
            new_token_values,
            gathered_keys,
            gathered_values,
            usable,
            owner_request,
        )

    adapters_all = adapter_table_row.shape[0]
    matches = request_adapter[0][:, None] == jnp.arange(adapters_all, dtype=jnp.int32)[None, :]
    chosen_pages = jnp.sum(jnp.where(matches, adapter_table_row[None, :], 0), axis=1)
    if SEPARATE_GATHER:
        adapter_in = jnp.concatenate(
            [lax.dynamic_slice_in_dim(down_everywhere, chosen_pages[r], 1, 0) for r in range(requests_here)]
        )
        adapter_out = jnp.concatenate(
            [lax.dynamic_slice_in_dim(up_everywhere, chosen_pages[r], 1, 0) for r in range(requests_here)]
        )
    else:
        selected = jnp.concatenate(
            [lax.dynamic_slice_in_dim(adapters_everywhere, chosen_pages[r], 1, 0) for r in range(requests_here)]
        )
        adapter_in = selected[:, :, :down_cols]
        adapter_out = selected[:, :, down_cols:]
    rank_size = adapter_in.shape[1]

    selector = (
        owner_request[:, None] == jnp.arange(requests_here, dtype=jnp.int32)[None, :]
    ).astype(jnp.float32)
    selector_half = selector.astype(jnp.bfloat16)
    base_part = jnp.dot(attention, output_weight, preferred_element_type=jnp.float32)
    low_terms = jnp.einsum("tc,rkc->trk", attention, adapter_in, preferred_element_type=jnp.float32)
    low_part = jnp.sum(low_terms * selector[:, :, None], axis=1)

    if TP_TRANSPOSED:
        base_t = jnp.einsum("tc,cw->wt", attention, output_weight, preferred_element_type=jnp.float32)
        base_slots = base_t.astype(jnp.bfloat16).reshape(groups, width_part, token_count)
        low_slots = jnp.broadcast_to(
            low_part.astype(jnp.bfloat16).T[None], (groups, rank_size, token_count)
        )
        slots = jnp.concatenate([base_slots, low_slots], axis=1)
        arrived = lax.all_to_all(slots, "tp", split_axis=0, concat_axis=0, tiled=True)
        arrived = jnp.sum(arrived.astype(jnp.float32), axis=0)
        base_local = arrived[:width_part].T
        low_sum = arrived[width_part:width_part + rank_size].T
    else:
        base_slots = base_part.astype(jnp.bfloat16).reshape(token_count, groups, width_part)
        base_slots = jnp.transpose(base_slots, (1, 0, 2))
        low_slots = jnp.broadcast_to(
            low_part.astype(jnp.bfloat16)[None], (groups, token_count, rank_size)
        )
        pad_cols = (-(width_part + rank_size)) % 128
        slots = jnp.concatenate(
            [base_slots, low_slots, jnp.zeros((groups, token_count, pad_cols), jnp.bfloat16)], axis=2
        )
        arrived = lax.all_to_all(slots, "tp", split_axis=0, concat_axis=0, tiled=True)
        arrived = arrived.astype(jnp.float32)
        base_local = jnp.sum(arrived[:, :, :width_part], axis=0)
        low_sum = jnp.sum(arrived[:, :, width_part:width_part + rank_size], axis=0)

    rows_masked = (low_sum.astype(jnp.bfloat16)[:, None, :] * selector_half[:, :, None]).reshape(
        token_count, requests_here * rank_size
    )
    projected = base_local + adapter_scale * jnp.dot(
        rows_masked,
        adapter_out.reshape(requests_here * rank_size, width_part),
        preferred_element_type=jnp.float32,
    )
    square_part = jnp.sum(projected * projected, axis=1)
    square_sum = lax.psum(square_part, "tp")
    mean_square = square_sum / (groups * width_part)
    scaled = projected * lax.rsqrt(mean_square + epsilon)[:, None]
    return (residual_input.astype(jnp.float32) + scaled * norm_scale_row).astype(jnp.bfloat16)


def solution(mesh):
    in_specs = (
        P("req", "tp"),
        P("req", "tp"),
        P("req", "tp"),
        P("req", "tp"),
        P("req", None, "tp"),
        P("req", None, "tp"),
        P("req", None),
        P("req", None),
        P("req", None),
        P("req", None),
        P(),
        P("tp", None),
        P("req", None, "tp"),
        P("req", None, "tp"),
        P("tp"),
    )
    out_specs = P("req", "tp")
    return jax.shard_map(local, mesh=mesh, in_specs=in_specs, out_specs=out_specs, check_vma=False)
```

```python
import jax
import jax.numpy as jnp
from jax import lax
from jax.sharding import PartitionSpec as P

HEAD_SIZE = 256
SEPARATE_GATHER = False
KV_OWNER_MAJOR = True
TP_TRANSPOSED = True
INDEX_TRANSPOSED = True


epsilon = 1e-06
adapter_scale = 2.0
masked_score = -1e30


def attend(
    query_rows, new_keys, new_values, gathered_keys, gathered_values, usable, owner_request
):
    token_count = query_rows.shape[0]
    kv_heads = new_keys.shape[1] // HEAD_SIZE
    group_size = query_rows.shape[1] // new_keys.shape[1]
    requests_here = gathered_keys.shape[0]
    cached_count = gathered_keys.shape[1]
    query_heads = query_rows.reshape(token_count, kv_heads, group_size, HEAD_SIZE)
    past_keys = gathered_keys.reshape(requests_here, cached_count, kv_heads, HEAD_SIZE)
    past_values = gathered_values.reshape(requests_here * cached_count, kv_heads, HEAD_SIZE)
    fresh_keys = new_keys.reshape(token_count, kv_heads, HEAD_SIZE)
    fresh_values = new_values.reshape(token_count, kv_heads, HEAD_SIZE)
    positions = jnp.arange(token_count, dtype=jnp.int32)
    scaling = HEAD_SIZE ** (-0.5)
    past_scores = (
        jnp.einsum("tgqd,rngd->tgqrn", query_heads, past_keys, preferred_element_type=jnp.float32)
        * scaling
    )
    past_mask = usable[None, :, :] & (
        owner_request[:, None, None] == jnp.arange(requests_here, dtype=jnp.int32)[None, :, None]
    )
    past_scores = jnp.where(past_mask[:, None, None, :, :], past_scores, masked_score)
    past_scores = past_scores.reshape(
        token_count, kv_heads, group_size, requests_here * cached_count
    )
    fresh_scores = (
        jnp.einsum("tgqd,ugd->tgqu", query_heads, fresh_keys, preferred_element_type=jnp.float32)
        * scaling
    )
    fresh_mask = (owner_request[:, None] == owner_request[None, :]) & (
        positions[None, :] <= positions[:, None]
    )
    fresh_scores = jnp.where(fresh_mask[:, None, None, :], fresh_scores, masked_score)
    scores = jnp.concatenate([past_scores, fresh_scores], axis=3)
    highest = jnp.max(scores, axis=3, keepdims=True)
    weights = jnp.exp(scores - highest)
    weights = (weights / jnp.sum(weights, axis=3, keepdims=True)).astype(jnp.bfloat16)
    all_values = jnp.concatenate([past_values, fresh_values], axis=0)
    mixed = jnp.einsum("tgqk,kgd->tgqd", weights, all_values, preferred_element_type=jnp.float32)
    return mixed.reshape(token_count, -1).astype(jnp.bfloat16)


def attend_flat(query_rows, new_keys, new_values, past_keys, past_values, past_mask, owner_request):
    token_count = query_rows.shape[0]
    kv_heads = new_keys.shape[1] // HEAD_SIZE
    group_size = query_rows.shape[1] // new_keys.shape[1]
    query_heads = query_rows.reshape(token_count, kv_heads, group_size, HEAD_SIZE)
    fresh_keys = new_keys.reshape(token_count, kv_heads, HEAD_SIZE)
    fresh_values = new_values.reshape(token_count, kv_heads, HEAD_SIZE)
    positions = jnp.arange(token_count, dtype=jnp.int32)
    scaling = HEAD_SIZE ** (-0.5)
    past_scores = (
        jnp.einsum("tgqd,kgd->tgqk", query_heads, past_keys, preferred_element_type=jnp.float32)
        * scaling
    )
    past_scores = jnp.where(past_mask[:, None, None, :], past_scores, masked_score)
    fresh_scores = (
        jnp.einsum("tgqd,ugd->tgqu", query_heads, fresh_keys, preferred_element_type=jnp.float32)
        * scaling
    )
    fresh_mask = (owner_request[:, None] == owner_request[None, :]) & (
        positions[None, :] <= positions[:, None]
    )
    fresh_scores = jnp.where(fresh_mask[:, None, None, :], fresh_scores, masked_score)
    scores = jnp.concatenate([past_scores, fresh_scores], axis=3)
    highest = jnp.max(scores, axis=3, keepdims=True)
    weights = jnp.exp(scores - highest)
    weights = (weights / jnp.sum(weights, axis=3, keepdims=True)).astype(jnp.bfloat16)
    all_values = jnp.concatenate([past_values, fresh_values], axis=0)
    mixed = jnp.einsum("tgqk,kgd->tgqd", weights, all_values, preferred_element_type=jnp.float32)
    return mixed.reshape(token_count, -1).astype(jnp.bfloat16)


def local(
    residual_input,
    new_token_queries,
    new_token_keys,
    new_token_values,
    key_page_pool,
    value_page_pool,
    request_page_table,
    page_token_length,
    request_token_length,
    request_adapter,
    adapter_table_row,
    output_weight,
    adapter_down_weight,
    adapter_up_weight,
    norm_scale_row,
):
    owners = lax.axis_size("req")
    groups = lax.axis_size("tp")
    requests_here = request_page_table.shape[0]
    page_rows = key_page_pool.shape[1]
    token_count = new_token_queries.shape[0]
    width_part = residual_input.shape[1]
    head_cols = key_page_pool.shape[2]
    down_cols = adapter_down_weight.shape[2]

    if SEPARATE_GATHER:
        down_everywhere, up_everywhere = lax.all_gather(
            (adapter_down_weight, adapter_up_weight), "req", axis=0, tiled=True
        )
    else:
        adapter_pair = jnp.concatenate([adapter_down_weight, adapter_up_weight], axis=2)
        adapters_everywhere = lax.all_gather(adapter_pair, "req", axis=0, tiled=True)

    if INDEX_TRANSPOSED:
        wanted = lax.all_to_all(request_page_table.T, "req", split_axis=0, concat_axis=0, tiled=True).T
    else:
        wanted = lax.all_to_all(request_page_table, "req", split_axis=1, concat_axis=1, tiled=True)
    page_picks = jnp.maximum(wanted, 0)
    kv_pool = jnp.concatenate([key_page_pool, value_page_pool], axis=2)
    lengths = request_token_length[0]
    positions = jnp.arange(token_count, dtype=jnp.int32)
    ends = jnp.cumsum(lengths)
    owner_request = jnp.sum((positions[:, None] >= ends[None, :]).astype(jnp.int32), axis=1)
    kv_heads = head_cols // HEAD_SIZE
    if KV_OWNER_MAJOR:
        kv_out = kv_pool[page_picks.T]
        kv_back = lax.all_to_all(kv_out, "req", split_axis=0, concat_axis=0, tiled=True)
        cached = owners * requests_here * page_rows
        past_keys = kv_back[..., :head_cols].reshape(cached, kv_heads, HEAD_SIZE)
        past_values = kv_back[..., head_cols:].reshape(cached, kv_heads, HEAD_SIZE)
        row_used = (
            jnp.arange(page_rows, dtype=jnp.int32)[None, None, :] < page_token_length.T[:, :, None]
        )
        request_match = owner_request[:, None] == jnp.arange(requests_here, dtype=jnp.int32)[None, :]
        past_mask = (row_used[None] & request_match[:, None, :, None]).reshape(token_count, cached)
        attention = attend_flat(
            new_token_queries,
            new_token_keys,
            new_token_values,
            past_keys,
            past_values,
            past_mask,
            owner_request,
        )
    else:
        kv_out = kv_pool[page_picks]
        kv_back = lax.all_to_all(kv_out, "req", split_axis=1, concat_axis=1, tiled=True)
        kv_back = kv_back.reshape(requests_here, owners * page_rows, 2 * head_cols)
        gathered_keys = kv_back[:, :, :head_cols]
        gathered_values = kv_back[:, :, head_cols:]
        usable = (
            jnp.arange(page_rows, dtype=jnp.int32)[None, None, :] < page_token_length[:, :, None]
        ).reshape(requests_here, owners * page_rows)
        attention = attend(
            new_token_queries,
            new_token_keys,
            new_token_values,
            gathered_keys,
            gathered_values,
            usable,
            owner_request,
        )

    adapters_all = adapter_table_row.shape[0]
    matches = request_adapter[0][:, None] == jnp.arange(adapters_all, dtype=jnp.int32)[None, :]
    chosen_pages = jnp.sum(jnp.where(matches, adapter_table_row[None, :], 0), axis=1)
    if SEPARATE_GATHER:
        adapter_in = jnp.concatenate(
            [lax.dynamic_slice_in_dim(down_everywhere, chosen_pages[r], 1, 0) for r in range(requests_here)]
        )
        adapter_out = jnp.concatenate(
            [lax.dynamic_slice_in_dim(up_everywhere, chosen_pages[r], 1, 0) for r in range(requests_here)]
        )
    else:
        selected = jnp.concatenate(
            [lax.dynamic_slice_in_dim(adapters_everywhere, chosen_pages[r], 1, 0) for r in range(requests_here)]
        )
        adapter_in = selected[:, :, :down_cols]
        adapter_out = selected[:, :, down_cols:]
    rank_size = adapter_in.shape[1]

    selector = (
        owner_request[:, None] == jnp.arange(requests_here, dtype=jnp.int32)[None, :]
    ).astype(jnp.float32)
    selector_half = selector.astype(jnp.bfloat16)
    base_part = jnp.dot(attention, output_weight, preferred_element_type=jnp.float32)
    low_terms = jnp.einsum("tc,rkc->trk", attention, adapter_in, preferred_element_type=jnp.float32)
    low_part = jnp.sum(low_terms * selector[:, :, None], axis=1)

    if TP_TRANSPOSED:
        base_t = jnp.einsum("tc,cw->wt", attention, output_weight, preferred_element_type=jnp.float32)
        base_slots = base_t.astype(jnp.bfloat16).reshape(groups, width_part, token_count)
        low_slots = jnp.broadcast_to(
            low_part.astype(jnp.bfloat16).T[None], (groups, rank_size, token_count)
        )
        slots = jnp.concatenate([base_slots, low_slots], axis=1)
        arrived = lax.all_to_all(slots, "tp", split_axis=0, concat_axis=0, tiled=True)
        arrived = jnp.sum(arrived.astype(jnp.float32), axis=0)
        base_local = arrived[:width_part].T
        low_sum = arrived[width_part:width_part + rank_size].T
    else:
        base_slots = base_part.astype(jnp.bfloat16).reshape(token_count, groups, width_part)
        base_slots = jnp.transpose(base_slots, (1, 0, 2))
        low_slots = jnp.broadcast_to(
            low_part.astype(jnp.bfloat16)[None], (groups, token_count, rank_size)
        )
        pad_cols = (-(width_part + rank_size)) % 128
        slots = jnp.concatenate(
            [base_slots, low_slots, jnp.zeros((groups, token_count, pad_cols), jnp.bfloat16)], axis=2
        )
        arrived = lax.all_to_all(slots, "tp", split_axis=0, concat_axis=0, tiled=True)
        arrived = arrived.astype(jnp.float32)
        base_local = jnp.sum(arrived[:, :, :width_part], axis=0)
        low_sum = jnp.sum(arrived[:, :, width_part:width_part + rank_size], axis=0)

    rows_masked = (low_sum.astype(jnp.bfloat16)[:, None, :] * selector_half[:, :, None]).reshape(
        token_count, requests_here * rank_size
    )
    projected = base_local + adapter_scale * jnp.dot(
        rows_masked,
        adapter_out.reshape(requests_here * rank_size, width_part),
        preferred_element_type=jnp.float32,
    )
    square_part = jnp.sum(projected * projected, axis=1)
    square_sum = jnp.sum(lax.all_gather(square_part, "tp", axis=0), axis=0)
    mean_square = square_sum / (groups * width_part)
    scaled = projected * lax.rsqrt(mean_square + epsilon)[:, None]
    return (residual_input.astype(jnp.float32) + scaled * norm_scale_row).astype(jnp.bfloat16)


def solution(mesh):
    in_specs = (
        P("req", "tp"),
        P("req", "tp"),
        P("req", "tp"),
        P("req", "tp"),
        P("req", None, "tp"),
        P("req", None, "tp"),
        P("req", None),
        P("req", None),
        P("req", None),
        P("req", None),
        P(),
        P("tp", None),
        P("req", None, "tp"),
        P("req", None, "tp"),
        P("tp"),
    )
    out_specs = P("req", "tp")
    return jax.shard_map(local, mesh=mesh, in_specs=in_specs, out_specs=out_specs, check_vma=False)
```

```python
import jax
import jax.numpy as jnp
from jax import lax
from jax.sharding import PartitionSpec as P

HEAD_SIZE = 256
SEPARATE_GATHER = False
KV_OWNER_MAJOR = True
TP_TRANSPOSED = True
INDEX_TRANSPOSED = True


epsilon = 1e-06
adapter_scale = 2.0
masked_score = -1e30


def attend(
    query_rows, new_keys, new_values, gathered_keys, gathered_values, usable, owner_request
):
    token_count = query_rows.shape[0]
    kv_heads = new_keys.shape[1] // HEAD_SIZE
    group_size = query_rows.shape[1] // new_keys.shape[1]
    requests_here = gathered_keys.shape[0]
    cached_count = gathered_keys.shape[1]
    query_heads = query_rows.reshape(token_count, kv_heads, group_size, HEAD_SIZE)
    past_keys = gathered_keys.reshape(requests_here, cached_count, kv_heads, HEAD_SIZE)
    past_values = gathered_values.reshape(requests_here * cached_count, kv_heads, HEAD_SIZE)
    fresh_keys = new_keys.reshape(token_count, kv_heads, HEAD_SIZE)
    fresh_values = new_values.reshape(token_count, kv_heads, HEAD_SIZE)
    positions = jnp.arange(token_count, dtype=jnp.int32)
    scaling = HEAD_SIZE ** (-0.5)
    past_scores = (
        jnp.einsum("tgqd,rngd->tgqrn", query_heads, past_keys, preferred_element_type=jnp.float32)
        * scaling
    )
    past_mask = usable[None, :, :] & (
        owner_request[:, None, None] == jnp.arange(requests_here, dtype=jnp.int32)[None, :, None]
    )
    past_scores = jnp.where(past_mask[:, None, None, :, :], past_scores, masked_score)
    past_scores = past_scores.reshape(
        token_count, kv_heads, group_size, requests_here * cached_count
    )
    fresh_scores = (
        jnp.einsum("tgqd,ugd->tgqu", query_heads, fresh_keys, preferred_element_type=jnp.float32)
        * scaling
    )
    fresh_mask = (owner_request[:, None] == owner_request[None, :]) & (
        positions[None, :] <= positions[:, None]
    )
    fresh_scores = jnp.where(fresh_mask[:, None, None, :], fresh_scores, masked_score)
    scores = jnp.concatenate([past_scores, fresh_scores], axis=3)
    highest = jnp.max(scores, axis=3, keepdims=True)
    weights = jnp.exp(scores - highest)
    weights = (weights / jnp.sum(weights, axis=3, keepdims=True)).astype(jnp.bfloat16)
    all_values = jnp.concatenate([past_values, fresh_values], axis=0)
    mixed = jnp.einsum("tgqk,kgd->tgqd", weights, all_values, preferred_element_type=jnp.float32)
    return mixed.reshape(token_count, -1).astype(jnp.bfloat16)


def attend_flat(query_rows, new_keys, new_values, past_keys, past_values, past_mask, owner_request):
    token_count = query_rows.shape[0]
    kv_heads = new_keys.shape[1] // HEAD_SIZE
    group_size = query_rows.shape[1] // new_keys.shape[1]
    query_heads = query_rows.reshape(token_count, kv_heads, group_size, HEAD_SIZE)
    fresh_keys = new_keys.reshape(token_count, kv_heads, HEAD_SIZE)
    fresh_values = new_values.reshape(token_count, kv_heads, HEAD_SIZE)
    positions = jnp.arange(token_count, dtype=jnp.int32)
    scaling = HEAD_SIZE ** (-0.5)
    past_scores = (
        jnp.einsum("tgqd,kgd->tgqk", query_heads, past_keys, preferred_element_type=jnp.float32)
        * scaling
    )
    past_scores = jnp.where(past_mask[:, None, None, :], past_scores, masked_score)
    fresh_scores = (
        jnp.einsum("tgqd,ugd->tgqu", query_heads, fresh_keys, preferred_element_type=jnp.float32)
        * scaling
    )
    fresh_mask = (owner_request[:, None] == owner_request[None, :]) & (
        positions[None, :] <= positions[:, None]
    )
    fresh_scores = jnp.where(fresh_mask[:, None, None, :], fresh_scores, masked_score)
    scores = jnp.concatenate([past_scores, fresh_scores], axis=3)
    highest = jnp.max(scores, axis=3, keepdims=True)
    weights = jnp.exp(scores - highest)
    weights = (weights / jnp.sum(weights, axis=3, keepdims=True)).astype(jnp.bfloat16)
    all_values = jnp.concatenate([past_values, fresh_values], axis=0)
    mixed = jnp.einsum("tgqk,kgd->tgqd", weights, all_values, preferred_element_type=jnp.float32)
    return mixed.reshape(token_count, -1).astype(jnp.bfloat16)


def local(
    residual_input,
    new_token_queries,
    new_token_keys,
    new_token_values,
    key_page_pool,
    value_page_pool,
    request_page_table,
    page_token_length,
    request_token_length,
    request_adapter,
    adapter_table_row,
    output_weight,
    adapter_down_weight,
    adapter_up_weight,
    norm_scale_row,
):
    owners = lax.axis_size("req")
    groups = lax.axis_size("tp")
    requests_here = request_page_table.shape[0]
    page_rows = key_page_pool.shape[1]
    token_count = new_token_queries.shape[0]
    width_part = residual_input.shape[1]
    head_cols = key_page_pool.shape[2]
    down_cols = adapter_down_weight.shape[2]

    if SEPARATE_GATHER:
        down_everywhere, up_everywhere = lax.all_gather(
            (adapter_down_weight, adapter_up_weight), "req", axis=0, tiled=True
        )
    else:
        adapter_pair = jnp.concatenate([adapter_down_weight, adapter_up_weight], axis=2)
        adapters_everywhere = lax.all_gather(adapter_pair, "req", axis=0, tiled=True)

    if INDEX_TRANSPOSED:
        wanted = lax.all_to_all(
            request_page_table.T.astype(jnp.bfloat16), "req", split_axis=0, concat_axis=0, tiled=True
        ).T.astype(jnp.int32)
    else:
        wanted = lax.all_to_all(request_page_table, "req", split_axis=1, concat_axis=1, tiled=True)
    page_picks = jnp.maximum(wanted, 0)
    kv_pool = jnp.concatenate([key_page_pool, value_page_pool], axis=2)
    lengths = request_token_length[0]
    positions = jnp.arange(token_count, dtype=jnp.int32)
    ends = jnp.cumsum(lengths)
    owner_request = jnp.sum((positions[:, None] >= ends[None, :]).astype(jnp.int32), axis=1)
    kv_heads = head_cols // HEAD_SIZE
    if KV_OWNER_MAJOR:
        kv_out = kv_pool[page_picks.T]
        kv_back = lax.all_to_all(kv_out, "req", split_axis=0, concat_axis=0, tiled=True)
        cached = owners * requests_here * page_rows
        past_keys = kv_back[..., :head_cols].reshape(cached, kv_heads, HEAD_SIZE)
        past_values = kv_back[..., head_cols:].reshape(cached, kv_heads, HEAD_SIZE)
        row_used = (
            jnp.arange(page_rows, dtype=jnp.int32)[None, None, :] < page_token_length.T[:, :, None]
        )
        request_match = owner_request[:, None] == jnp.arange(requests_here, dtype=jnp.int32)[None, :]
        past_mask = (row_used[None] & request_match[:, None, :, None]).reshape(token_count, cached)
        attention = attend_flat(
            new_token_queries,
            new_token_keys,
            new_token_values,
            past_keys,
            past_values,
            past_mask,
            owner_request,
        )
    else:
        kv_out = kv_pool[page_picks]
        kv_back = lax.all_to_all(kv_out, "req", split_axis=1, concat_axis=1, tiled=True)
        kv_back = kv_back.reshape(requests_here, owners * page_rows, 2 * head_cols)
        gathered_keys = kv_back[:, :, :head_cols]
        gathered_values = kv_back[:, :, head_cols:]
        usable = (
            jnp.arange(page_rows, dtype=jnp.int32)[None, None, :] < page_token_length[:, :, None]
        ).reshape(requests_here, owners * page_rows)
        attention = attend(
            new_token_queries,
            new_token_keys,
            new_token_values,
            gathered_keys,
            gathered_values,
            usable,
            owner_request,
        )

    adapters_all = adapter_table_row.shape[0]
    matches = request_adapter[0][:, None] == jnp.arange(adapters_all, dtype=jnp.int32)[None, :]
    chosen_pages = jnp.sum(jnp.where(matches, adapter_table_row[None, :], 0), axis=1)
    if SEPARATE_GATHER:
        adapter_in = jnp.concatenate(
            [lax.dynamic_slice_in_dim(down_everywhere, chosen_pages[r], 1, 0) for r in range(requests_here)]
        )
        adapter_out = jnp.concatenate(
            [lax.dynamic_slice_in_dim(up_everywhere, chosen_pages[r], 1, 0) for r in range(requests_here)]
        )
    else:
        selected = jnp.concatenate(
            [lax.dynamic_slice_in_dim(adapters_everywhere, chosen_pages[r], 1, 0) for r in range(requests_here)]
        )
        adapter_in = selected[:, :, :down_cols]
        adapter_out = selected[:, :, down_cols:]
    rank_size = adapter_in.shape[1]

    selector = (
        owner_request[:, None] == jnp.arange(requests_here, dtype=jnp.int32)[None, :]
    ).astype(jnp.float32)
    selector_half = selector.astype(jnp.bfloat16)
    base_part = jnp.dot(attention, output_weight, preferred_element_type=jnp.float32)
    low_terms = jnp.einsum("tc,rkc->trk", attention, adapter_in, preferred_element_type=jnp.float32)
    low_part = jnp.sum(low_terms * selector[:, :, None], axis=1)

    if TP_TRANSPOSED:
        base_t = jnp.einsum("tc,cw->wt", attention, output_weight, preferred_element_type=jnp.float32)
        base_slots = base_t.astype(jnp.bfloat16).reshape(groups, width_part, token_count)
        low_slots = jnp.broadcast_to(
            low_part.astype(jnp.bfloat16).T[None], (groups, rank_size, token_count)
        )
        slots = jnp.concatenate([base_slots, low_slots], axis=1)
        arrived = lax.all_to_all(slots, "tp", split_axis=0, concat_axis=0, tiled=True)
        arrived = jnp.sum(arrived.astype(jnp.float32), axis=0)
        base_local = arrived[:width_part].T
        low_sum = arrived[width_part:width_part + rank_size].T
    else:
        base_slots = base_part.astype(jnp.bfloat16).reshape(token_count, groups, width_part)
        base_slots = jnp.transpose(base_slots, (1, 0, 2))
        low_slots = jnp.broadcast_to(
            low_part.astype(jnp.bfloat16)[None], (groups, token_count, rank_size)
        )
        pad_cols = (-(width_part + rank_size)) % 128
        slots = jnp.concatenate(
            [base_slots, low_slots, jnp.zeros((groups, token_count, pad_cols), jnp.bfloat16)], axis=2
        )
        arrived = lax.all_to_all(slots, "tp", split_axis=0, concat_axis=0, tiled=True)
        arrived = arrived.astype(jnp.float32)
        base_local = jnp.sum(arrived[:, :, :width_part], axis=0)
        low_sum = jnp.sum(arrived[:, :, width_part:width_part + rank_size], axis=0)

    rows_masked = (low_sum.astype(jnp.bfloat16)[:, None, :] * selector_half[:, :, None]).reshape(
        token_count, requests_here * rank_size
    )
    projected = base_local + adapter_scale * jnp.dot(
        rows_masked,
        adapter_out.reshape(requests_here * rank_size, width_part),
        preferred_element_type=jnp.float32,
    )
    square_part = jnp.sum(projected * projected, axis=1)
    square_sum = jnp.sum(lax.all_gather(square_part, "tp", axis=0), axis=0)
    mean_square = square_sum / (groups * width_part)
    scaled = projected * lax.rsqrt(mean_square + epsilon)[:, None]
    return (residual_input.astype(jnp.float32) + scaled * norm_scale_row).astype(jnp.bfloat16)


def solution(mesh):
    in_specs = (
        P("req", "tp"),
        P("req", "tp"),
        P("req", "tp"),
        P("req", "tp"),
        P("req", None, "tp"),
        P("req", None, "tp"),
        P("req", None),
        P("req", None),
        P("req", None),
        P("req", None),
        P(),
        P("tp", None),
        P("req", None, "tp"),
        P("req", None, "tp"),
        P("tp"),
    )
    out_specs = P("req", "tp")
    return jax.shard_map(local, mesh=mesh, in_specs=in_specs, out_specs=out_specs, check_vma=False)
```
